512 devices in a mesh: own: 64 (over z, y), rep: 8 (over x, core).
Axes of the slice: x: 4, y: 8, z: 8, core: 2. Of those that a mesh axis runs over, the one named last changes fastest.
Arguments:
- tokens: bfloat16 [65536, 2560], P(('own', 'rep')), may hold values from -6 to 6
- cotangent: bfloat16 [65536, 2560], P(('own', 'rep')), may hold values from -6 to 6
- route: int32 [65536, 6], P(('own', 'rep')), may hold values from 0 to 159, all different within a row; in each aligned block of 128 rows (0 to 127, 128 to 255, ...) at most 6 rows name the same one
- gate_index: int32 [65536, 6], P(('own', 'rep')), may hold values from 0 to 255
- gate_table: float32 [256], replicated, may hold values from 0.1 to 1
- w_gate: bfloat16 [16384, 2560], P(('own', 'rep')), may hold values from -0.125 to 0.125
- w_up: bfloat16 [16384, 2560], P(('own', 'rep')), may hold values from -0.125 to 0.125
- w_down: bfloat16 [16384, 2560], P(('own', 'rep')), may hold values from -0.1875 to 0.1875
Outputs:
- grad_tokens: bfloat16 [65536, 2560], P(('own', 'rep'))
- grad_w_gate: float32 [16384, 2560], P(('own', 'rep'))
- grad_w_up: float32 [16384, 2560], P(('own', 'rep'))
- grad_w_down: float32 [16384, 2560], P(('own', 'rep'))
The draws below stay inside these ranges and needn't reach their ends.
Inputs may be any that keep to these rules, and one draw needn't show every extreme that they name: `route`: each row names 6 different experts. Among the rows of one device no expert is named by more than 6 rows, and in some device some expert is named by exactly 6.
All inputs are finite; a program needn't handle non-finite values.
Results may differ from the reference program's by a relative error of at most 0.015.
Values may be sent and summed in bfloat16 or wider, within the bound.
No kernel may reach another device: no remote copies, remote signals or barrier semaphores. Data moves between devices by JAX's collectives and lax.ppermute only.
A program may use at most 64 MiB of HBM per device.

```python
import math
import jax
import jax.numpy as jnp
import numpy as np
from jax import lax

D = 2560
FF = 1024
EXPERTS = 160
TOP = 6
SPLIT = 4
GTAB = 256
TOK_DEV = 128
CAP = 6
EW = 16
TOKENS = 65536
N_OWN = 64
N_REP = 8


def touch_ends(values, rng, smallest, top_value):
    extent = values.shape
    index_at = [jax.random.randint(jax.random.fold_in(rng, axis), (), 0, extent[axis]) for axis in range(len(extent))]
    values = values.at[tuple(index_at)].set(smallest)
    longest = extent.index(max(extent))
    index_at[longest] = (index_at[longest] + 1) % extent[longest]
    return values.at[tuple(index_at)].set(top_value)


def block_levels(rng, extent, split, least, top_value):
    def one(dim, parts):
        steps = jax.random.uniform(jax.random.fold_in(jax.random.fold_in(rng, 6), dim), (parts,), jnp.float32, least / len(split), top_value / len(split))
        return jnp.repeat(jnp.exp(steps), extent[dim] // parts).reshape((-1,) + (1,) * (len(extent) - dim - 1))

    loudness = one(*split[0])
    for cut in split[1:]:
        loudness = loudness * one(*cut)
    return loudness


def shared_out(own_key, own, number, rows, number_of, top, reach, skew):
    sequence = jax.random.permutation(own_key, number_of)
    heavy_load, usual = shares(number_of, rows * top, reach, skew, True), shares(number_of, rows * top, reach, skew, False)
    places = jnp.arange(number_of)

    def named(tallies, rotation):
        used = int((tallies > 0).sum())
        fixed = max(1, used // 4)
        moved = fixed + (places - fixed + rotation * (used - fixed)) % max(1, number_of - fixed)
        return jnp.zeros((number_of,), jnp.int32).at[sequence[jnp.where(places < fixed, places, moved)]].set(jnp.asarray(tallies, jnp.int32))

    tallies = jnp.where(number % 4 == 0, named(heavy_load, number // 4), named(usual, number - number // 4 - 1))
    mixed = jax.random.permutation(jax.random.fold_in(own, 3), number_of)
    donor, receiver = mixed[0:number_of // 2 * 2:2], mixed[1:number_of // 2 * 2:2]
    slack = jnp.minimum(tallies[donor] - 1, reach - tallies[receiver]) // 2
    slack = jnp.where((donor == sequence[0]) | (receiver == sequence[0]) | (tallies[receiver] == 0), 0, jnp.maximum(slack, 0))
    moved = jax.random.randint(jax.random.fold_in(own, 4), (number_of // 2,), 0, 1 << 20) % (slack + 1)
    tallies = tallies.at[donor].add(-moved).at[receiver].add(moved)
    labels = jnp.searchsorted(jnp.cumsum(tallies), jnp.arange(rows * top), side="right").astype(jnp.int32)
    grid = labels.reshape(top, rows).T
    grid = grid[jax.random.permutation(jax.random.fold_in(own, 1), rows)]
    rotation = jax.random.randint(jax.random.fold_in(own, 2), (rows, 1), 0, top)
    return jnp.take_along_axis(grid, (jnp.arange(top)[None, :] + rotation) % top, axis=1)


def shares(number_of, total, reach, lean, full):
    portions = [(1 << 20) // math.isqrt(rank ** lean) + 1 for rank in range(1, number_of + 1)]
    largest = reach if full else min(reach, max(-(-total // number_of), total * portions[0] // sum(portions)))
    least = 1 if total - largest >= number_of - 1 else 0
    counts, spare = [largest] + [least] * (number_of - 1), total - largest - least * (number_of - 1)
    while spare > 0:
        candidates = [i for i in range(1, number_of) if counts[i] < largest] or [i for i in range(1, number_of) if counts[i] < reach]
        pool, budget = sum([portions[i] for i in candidates]), spare
        for i in candidates:
            extra = min(reach - counts[i], max(1, budget * portions[i] // pool), spare)
            counts[i] = counts[i] + extra
            spare = spare - extra
    return np.array(counts)


def gaussian(own_key, dims, spread, reach, pieces=(), kind=jnp.bfloat16):
    drawn = jax.random.normal(own_key, dims, jnp.float32) * spread
    if len(pieces) > 0:
        drawn = block_levels(own_key, dims, pieces, -0.22, 0.18) * drawn
    return jnp.clip(drawn, min=-reach, max=reach).astype(kind)


def setup_inputs(seed: int = 0) -> dict:
    streams_of = jax.random.split(jax.random.key(seed), 9)
    tokens = gaussian(streams_of[0], (TOKENS, D), 1.0, 6.0, ((0, 512),))
    cotangent = gaussian(streams_of[1], (TOKENS, D), 1.0, 6.0, ((0, 512),))
    route_keys = jax.random.split(jax.random.fold_in(streams_of[2], 1), TOKENS // TOK_DEV)
    route_turns = jax.random.permutation(jax.random.fold_in(streams_of[2], 3), TOKENS // TOK_DEV)
    route = jax.vmap(lambda own, number: shared_out(jax.random.fold_in(streams_of[2], 2), own, number, TOK_DEV, EXPERTS, TOP, CAP, 2))(route_keys, route_turns).reshape((TOKENS, TOP))
    gate_index = touch_ends(jax.random.randint(streams_of[3], (TOKENS, TOP), 0, GTAB), jax.random.fold_in(streams_of[3], 1), 0, GTAB - 1).astype(jnp.int32)
    gate_table = jnp.clip(jnp.exp(jax.random.uniform(streams_of[4], (GTAB,), jnp.float32, math.log(0.1), math.log(1.0))), 0.1, 1.0)
    w_gate = gaussian(streams_of[5], (EW * FF, D), D ** -0.5, 0.125, ((0, 512),))
    w_up = gaussian(streams_of[6], (EW * FF, D), D ** -0.5, 0.125, ((0, 512),))
    w_down = gaussian(streams_of[7], (EW * FF, D), FF ** -0.5, 0.1875, ((0, 512),))
    return dict(tokens=tokens, cotangent=cotangent, route=route, gate_index=gate_index, gate_table=gate_table, w_gate=w_gate, w_up=w_up, w_down=w_down)


def silu_parts(pre_gate):
    sigmoid_value = jax.nn.sigmoid(pre_gate)
    return pre_gate * sigmoid_value, sigmoid_value * (1.0 + pre_gate * (1.0 - sigmoid_value))


def rep_partials(left_rows, right_rows):
    left_grid = left_rows.reshape(N_OWN, N_REP, CAP, left_rows.shape[-1]).astype(jnp.float32)
    right_grid = right_rows.reshape(N_OWN, N_REP, CAP, right_rows.shape[-1]).astype(jnp.float32)
    partials = jnp.einsum('orcf,orcd->rfd', left_grid, right_grid, precision=lax.Precision.HIGHEST)
    return lax.optimization_barrier(partials.astype(jnp.bfloat16)).astype(jnp.float32).sum(axis=0)


def block_sums(delta_rows, panel):
    delta_blocks = delta_rows.astype(jnp.float32).reshape(delta_rows.shape[0], SPLIT, FF // SPLIT)
    panel_blocks = panel.astype(jnp.float32).reshape(SPLIT, FF // SPLIT, D)
    return jnp.einsum('rsf,sfd->rsd', delta_blocks, panel_blocks, precision=lax.Precision.HIGHEST)


def reference(tokens, cotangent, route, gate_index, gate_table, w_gate, w_up, w_down):
    devices_all = N_OWN * N_REP
    window = N_OWN // SPLIT
    gate_values = gate_table[gate_index].reshape(devices_all, TOK_DEV * TOP)
    routes = route.reshape(devices_all, TOK_DEV * TOP)
    expert_ids = jnp.arange(window, dtype=jnp.int32)
    slot_ids = jnp.arange(CAP, dtype=jnp.int32)
    is_named = (routes[:, :, None] == expert_ids[None, None, :]).astype(jnp.int32)
    earlier = jnp.cumsum(is_named, axis=1) - is_named
    slot_hits = (is_named[:, :, :, None] * (earlier[:, :, :, None] == slot_ids[None, None, None, :]).astype(jnp.int32)).astype(jnp.float32)
    select = slot_hits.reshape(devices_all, TOK_DEV, TOP, window, CAP).sum(axis=2)
    slot_gate = jnp.einsum('npec,np->enc', slot_hits, gate_values, precision=lax.Precision.HIGHEST)
    token_rows = tokens.reshape(devices_all, TOK_DEV, D).astype(jnp.float32)
    cot_rows = cotangent.reshape(devices_all, TOK_DEV, D).astype(jnp.float32)
    sent_x = jnp.einsum('ntec,ntd->encd', select, token_rows, precision=lax.Precision.HIGHEST).astype(jnp.bfloat16)
    sent_dy = jnp.einsum('ntec,ntd->encd', select, cot_rows, precision=lax.Precision.HIGHEST)
    sent_cot = (slot_gate[:, :, :, None] * sent_dy).astype(jnp.bfloat16)
    select_first = jnp.transpose(select, (2, 0, 1, 3))
    gate_rows = w_gate.reshape(window, FF, D)
    up_rows = w_up.reshape(window, FF, D)
    down_rows = w_down.reshape(window, FF, D)

    def per_expert(accumulated, inputs):
        expert_x, expert_cot, expert_pick, expert_gate, expert_up, expert_down = inputs
        rows_x = expert_x.reshape(-1, D)
        rows_cot = expert_cot.reshape(-1, D)
        pre_gate = jnp.dot(rows_x, expert_gate.T, preferred_element_type=jnp.float32)
        pre_up = jnp.dot(rows_x, expert_up.T, preferred_element_type=jnp.float32)
        active, slope_value = silu_parts(pre_gate)
        hidden = (active * pre_up).astype(jnp.bfloat16)
        hidden_delta = jnp.dot(rows_cot, expert_down.T, preferred_element_type=jnp.float32)
        gate_delta = (hidden_delta * pre_up * slope_value).astype(jnp.bfloat16)
        up_delta = (hidden_delta * active).astype(jnp.bfloat16)
        block_grad = block_sums(gate_delta, expert_gate) + block_sums(up_delta, expert_up)
        grad_rows = lax.optimization_barrier(block_grad.astype(jnp.bfloat16)).astype(jnp.float32).sum(axis=1)
        accumulated = accumulated + jnp.einsum('ntc,ncd->ntd', expert_pick, grad_rows.reshape(devices_all, CAP, D), precision=lax.Precision.HIGHEST)
        return accumulated, (rep_partials(gate_delta, rows_x), rep_partials(up_delta, rows_x), rep_partials(hidden, rows_cot))

    start_value = jnp.zeros((devices_all, TOK_DEV, D), jnp.float32)
    accumulated, weight_grads = lax.scan(per_expert, start_value, (sent_x, sent_cot, select_first, gate_rows, up_rows, down_rows))
    grad_tokens = accumulated.reshape(devices_all * TOK_DEV, D).astype(jnp.bfloat16)
    return (grad_tokens, weight_grads[0].reshape(window * FF, D), weight_grads[1].reshape(window * FF, D), weight_grads[2].reshape(window * FF, D))
```

```python
import jax
import jax.numpy as jnp
from jax import lax
from jax.sharding import PartitionSpec as P

SPLIT = 4
CAP = 6


def silu_parts(pre_gate):
    sigmoid_value = jax.nn.sigmoid(pre_gate)
    return (pre_gate * sigmoid_value, sigmoid_value * (1.0 + pre_gate * (1.0 - sigmoid_value)))


def panel_terms(rows_x, rows_cot, panel_gate, panel_up, panel_down):
    pre_gate = jnp.dot(rows_x, panel_gate.T, preferred_element_type=jnp.float32)
    pre_up = jnp.dot(rows_x, panel_up.T, preferred_element_type=jnp.float32)
    active, slope_value = silu_parts(pre_gate)
    hidden = (active * pre_up).astype(jnp.bfloat16)
    hidden_delta = jnp.dot(rows_cot, panel_down.T, preferred_element_type=jnp.float32)
    gate_delta = (hidden_delta * pre_up * slope_value).astype(jnp.bfloat16)
    up_delta = (hidden_delta * active).astype(jnp.bfloat16)
    grad_rows = jnp.dot(gate_delta, panel_gate, preferred_element_type=jnp.float32) + jnp.dot(
        up_delta, panel_up, preferred_element_type=jnp.float32
    )
    grad_gate = jnp.dot(gate_delta.T, rows_x, preferred_element_type=jnp.float32)
    grad_up = jnp.dot(up_delta.T, rows_x, preferred_element_type=jnp.float32)
    grad_down = jnp.dot(hidden.T, rows_cot, preferred_element_type=jnp.float32)
    return (grad_rows, grad_gate, grad_up, grad_down)


def slot_tables(route, gate_index, gate_table, experts_here):
    tok_count, choices_each = route.shape
    slots = experts_here * CAP
    column = jnp.arange(slots, dtype=jnp.int32)[None, :]
    pair_route = route.reshape(-1)[:, None]
    is_named = (pair_route == column // CAP).astype(jnp.int32)
    earlier = jnp.cumsum(is_named, axis=0) - is_named
    hit = jnp.where(earlier == column % CAP, is_named, 0)
    gate_values = jnp.take(gate_table, gate_index.reshape(-1), axis=0)
    slot_gate = jnp.sum(jnp.where(hit > 0, gate_values[:, None], 0.0), axis=0)
    select = hit.reshape(tok_count, choices_each, slots).sum(axis=1).astype(jnp.float32)
    return select, slot_gate


def per_device(tokens, cotangent, route, gate_index, gate_table, w_gate, w_up, w_down):
    owners = lax.axis_size("own")
    experts_here = owners // SPLIT
    model_width = tokens.shape[1]
    select, slot_gate = slot_tables(route, gate_index, gate_table, experts_here)
    picker = select.astype(jnp.bfloat16)
    sent_x = jnp.dot(picker.T, tokens, preferred_element_type=jnp.float32).astype(jnp.bfloat16)
    sent_dy = jnp.dot(picker.T, cotangent, preferred_element_type=jnp.float32)
    sent_cot = (slot_gate[:, None] * sent_dy).astype(jnp.bfloat16)

    both = jnp.concatenate(
        [sent_x.reshape(experts_here, 1, CAP, model_width), sent_cot.reshape(experts_here, 1, CAP, model_width)],
        axis=2,
    )
    spread = jnp.broadcast_to(both, (experts_here, SPLIT, 2 * CAP, model_width)).reshape(
        owners, 2 * CAP, model_width
    )
    got = lax.all_to_all(spread, "own", split_axis=0, concat_axis=0, tiled=True)
    rows_x = got[:, :CAP].reshape(owners * CAP, model_width)
    rows_cot = got[:, CAP:].reshape(owners * CAP, model_width)
    full_gate, full_up, full_down = (
        lax.all_gather(w_gate, "rep", axis=0, tiled=True),
        lax.all_gather(w_up, "rep", axis=0, tiled=True),
        lax.all_gather(w_down, "rep", axis=0, tiled=True),
    )
    grad_rows, grad_gate, grad_up, grad_down = panel_terms(
        rows_x, rows_cot, full_gate, full_up, full_down
    )
    block_rows = grad_rows.astype(jnp.bfloat16).reshape(owners, CAP, model_width)
    returned = lax.all_to_all(block_rows, "own", split_axis=0, concat_axis=0, tiled=True)
    per_slot = (
        returned.astype(jnp.float32)
        .reshape(experts_here, SPLIT, CAP, model_width)
        .sum(axis=1)
        .reshape(experts_here * CAP, model_width)
    )
    grad_tokens = jnp.dot(
        select, per_slot, precision=lax.Precision.HIGHEST, preferred_element_type=jnp.float32
    ).astype(jnp.bfloat16)
    stacked = jnp.stack([grad_gate, grad_up, grad_down]).astype(jnp.bfloat16)
    shares = lax.psum_scatter(stacked, "rep", scatter_dimension=1, tiled=True).astype(jnp.float32)
    return (grad_tokens, shares[0], shares[1], shares[2])


def solution(mesh):
    return jax.shard_map(
        per_device,
        mesh=mesh,
        in_specs=(
            P(("own", "rep"), None),
            P(("own", "rep"), None),
            P(("own", "rep"), None),
            P(("own", "rep"), None),
            P(),
            P(("own", "rep"), None),
            P(("own", "rep"), None),
            P(("own", "rep"), None),
        ),
        out_specs=(
            P(("own", "rep"), None),
            P(("own", "rep"), None),
            P(("own", "rep"), None),
            P(("own", "rep"), None),
        ),
        check_vma=False,
    )
```

```python
import jax
import jax.numpy as jnp
from jax import lax
from jax.sharding import PartitionSpec as P

SPLIT = 4
CAP = 6


def silu_parts(pre_gate):
    sigmoid_value = jax.nn.sigmoid(pre_gate)
    return (pre_gate * sigmoid_value, sigmoid_value * (1.0 + pre_gate * (1.0 - sigmoid_value)))


def panel_terms(rows_x, rows_cot, panel_gate, panel_up, panel_down):
    pre_gate = jnp.dot(rows_x, panel_gate.T, preferred_element_type=jnp.float32)
    pre_up = jnp.dot(rows_x, panel_up.T, preferred_element_type=jnp.float32)
    active, slope_value = silu_parts(pre_gate)
    hidden = (active * pre_up).astype(jnp.bfloat16)
    hidden_delta = jnp.dot(rows_cot, panel_down.T, preferred_element_type=jnp.float32)
    gate_delta = (hidden_delta * pre_up * slope_value).astype(jnp.bfloat16)
    up_delta = (hidden_delta * active).astype(jnp.bfloat16)
    grad_rows = jnp.dot(gate_delta, panel_gate, preferred_element_type=jnp.float32) + jnp.dot(
        up_delta, panel_up, preferred_element_type=jnp.float32
    )
    grad_gate = jnp.dot(gate_delta.T, rows_x, preferred_element_type=jnp.float32)
    grad_up = jnp.dot(up_delta.T, rows_x, preferred_element_type=jnp.float32)
    grad_down = jnp.dot(hidden.T, rows_cot, preferred_element_type=jnp.float32)
    return (grad_rows, grad_gate, grad_up, grad_down)


def slot_tables(route, gate_index, gate_table, experts_here):
    tok_count, choices_each = route.shape
    slots = experts_here * CAP
    column = jnp.arange(slots, dtype=jnp.int32)[None, :]
    pair_route = route.reshape(-1)[:, None]
    is_named = (pair_route == column // CAP).astype(jnp.int32)
    earlier = jnp.cumsum(is_named, axis=0) - is_named
    hit = jnp.where(earlier == column % CAP, is_named, 0)
    gate_values = jnp.take(gate_table, gate_index.reshape(-1), axis=0)
    slot_gate = jnp.sum(jnp.where(hit > 0, gate_values[:, None], 0.0), axis=0)
    select = hit.reshape(tok_count, choices_each, slots).sum(axis=1).astype(jnp.float32)
    return select, slot_gate


def per_device(tokens, cotangent, route, gate_index, gate_table, w_gate, w_up, w_down):
    owners = lax.axis_size("own")
    experts_here = owners // SPLIT
    model_width = tokens.shape[1]
    select, slot_gate = slot_tables(route, gate_index, gate_table, experts_here)
    picker = select.astype(jnp.bfloat16)
    sent_x = jnp.dot(picker.T, tokens, preferred_element_type=jnp.float32).astype(jnp.bfloat16)
    sent_dy = jnp.dot(picker.T, cotangent, preferred_element_type=jnp.float32)
    sent_cot = (slot_gate[:, None] * sent_dy).astype(jnp.bfloat16)

    both = jnp.concatenate(
        [sent_x.reshape(experts_here, 1, CAP, model_width), sent_cot.reshape(experts_here, 1, CAP, model_width)],
        axis=2,
    )
    spread = jnp.broadcast_to(both, (experts_here, SPLIT, 2 * CAP, model_width)).reshape(
        owners, 16, -1
    )
    got = lax.all_to_all(spread, "own", split_axis=0, concat_axis=0, tiled=True)
    got = got.reshape(owners, 2 * CAP, model_width)
    rows_x = got[:, :CAP].reshape(owners * CAP, model_width)
    rows_cot = got[:, CAP:].reshape(owners * CAP, model_width)
    full_gate, full_up, full_down = (
        lax.all_gather(w_gate, "rep", axis=0, tiled=True),
        lax.all_gather(w_up, "rep", axis=0, tiled=True),
        lax.all_gather(w_down, "rep", axis=0, tiled=True),
    )
    grad_rows, grad_gate, grad_up, grad_down = panel_terms(
        rows_x, rows_cot, full_gate, full_up, full_down
    )
    block_rows = grad_rows.astype(jnp.bfloat16).reshape(owners, 16, -1)
    returned = lax.all_to_all(block_rows, "own", split_axis=0, concat_axis=0, tiled=True)
    per_slot = (
        returned.reshape(owners, CAP, model_width).astype(jnp.float32)
        .reshape(experts_here, SPLIT, CAP, model_width)
        .sum(axis=1)
        .reshape(experts_here * CAP, model_width)
    )
    grad_tokens = jnp.dot(
        select, per_slot, precision=lax.Precision.HIGHEST, preferred_element_type=jnp.float32
    ).astype(jnp.bfloat16)
    stacked = jnp.stack([grad_gate, grad_up, grad_down]).astype(jnp.bfloat16)
    shares = lax.psum_scatter(stacked, "rep", scatter_dimension=1, tiled=True).astype(jnp.float32)
    return (grad_tokens, shares[0], shares[1], shares[2])


def solution(mesh):
    return jax.shard_map(
        per_device,
        mesh=mesh,
        in_specs=(
            P(("own", "rep"), None),
            P(("own", "rep"), None),
            P(("own", "rep"), None),
            P(("own", "rep"), None),
            P(),
            P(("own", "rep"), None),
            P(("own", "rep"), None),
            P(("own", "rep"), None),
        ),
        out_specs=(
            P(("own", "rep"), None),
            P(("own", "rep"), None),
            P(("own", "rep"), None),
            P(("own", "rep"), None),
        ),
        check_vma=False,
    )
```

```python
import jax
import jax.numpy as jnp
from jax import lax
from jax.sharding import PartitionSpec as P

SPLIT = 4
CAP = 6


def silu_parts(pre_gate):
    sigmoid_value = jax.nn.sigmoid(pre_gate)
    return (pre_gate * sigmoid_value, sigmoid_value * (1.0 + pre_gate * (1.0 - sigmoid_value)))


def panel_terms(rows_x, rows_cot, panel_gate, panel_up, panel_down):
    pre_gate = jnp.dot(rows_x, panel_gate.T, preferred_element_type=jnp.float32)
    pre_up = jnp.dot(rows_x, panel_up.T, preferred_element_type=jnp.float32)
    active, slope_value = silu_parts(pre_gate)
    hidden = (active * pre_up).astype(jnp.bfloat16)
    hidden_delta = jnp.dot(rows_cot, panel_down.T, preferred_element_type=jnp.float32)
    gate_delta = (hidden_delta * pre_up * slope_value).astype(jnp.bfloat16)
    up_delta = (hidden_delta * active).astype(jnp.bfloat16)
    grad_rows = jnp.dot(gate_delta, panel_gate, preferred_element_type=jnp.float32) + jnp.dot(
        up_delta, panel_up, preferred_element_type=jnp.float32
    )
    grad_gate = jnp.dot(gate_delta.T, rows_x, preferred_element_type=jnp.float32)
    grad_up = jnp.dot(up_delta.T, rows_x, preferred_element_type=jnp.float32)
    grad_down = jnp.dot(hidden.T, rows_cot, preferred_element_type=jnp.float32)
    return (grad_rows, grad_gate, grad_up, grad_down)


def slot_tables(route, gate_index, gate_table, experts_here):
    tok_count, choices_each = route.shape
    slots = experts_here * CAP
    column = jnp.arange(slots, dtype=jnp.int32)[None, :]
    pair_route = route.reshape(-1)[:, None]
    is_named = (pair_route == column // CAP).astype(jnp.int32)
    earlier = jnp.cumsum(is_named, axis=0) - is_named
    hit = jnp.where(earlier == column % CAP, is_named, 0)
    gate_values = jnp.take(gate_table, gate_index.reshape(-1), axis=0)
    slot_gate = jnp.sum(jnp.where(hit > 0, gate_values[:, None], 0.0), axis=0)
    select = hit.reshape(tok_count, choices_each, slots).sum(axis=1).astype(jnp.float32)
    return select, slot_gate


def per_device(tokens, cotangent, route, gate_index, gate_table, w_gate, w_up, w_down):
    owners = lax.axis_size("own")
    experts_here = owners // SPLIT
    model_width = tokens.shape[1]
    select, slot_gate = slot_tables(route, gate_index, gate_table, experts_here)
    picker = select.astype(jnp.bfloat16)
    sent_x = jnp.dot(picker.T, tokens, preferred_element_type=jnp.float32).astype(jnp.bfloat16)
    sent_dy = jnp.dot(picker.T, cotangent, preferred_element_type=jnp.float32)
    sent_cot = (slot_gate[:, None] * sent_dy).astype(jnp.bfloat16)

    both = jnp.concatenate(
        [sent_x.reshape(experts_here, CAP, model_width), sent_cot.reshape(experts_here, CAP, model_width)],
        axis=1,
    ).reshape(experts_here, 1, 16, -1)
    spread = jnp.broadcast_to(both, (experts_here, SPLIT) + both.shape[2:]).reshape(owners, 16, -1)
    got = lax.all_to_all(spread, "own", split_axis=0, concat_axis=0, tiled=True)
    rows_x = got[:, :8].reshape(owners * CAP, model_width)
    rows_cot = got[:, 8:].reshape(owners * CAP, model_width)
    full_gate, full_up, full_down = (
        lax.all_gather(w_gate, "rep", axis=0, tiled=True),
        lax.all_gather(w_up, "rep", axis=0, tiled=True),
        lax.all_gather(w_down, "rep", axis=0, tiled=True),
    )
    grad_rows, grad_gate, grad_up, grad_down = panel_terms(
        rows_x, rows_cot, full_gate, full_up, full_down
    )
    block_rows = grad_rows.astype(jnp.bfloat16).reshape(owners, 16, -1)
    returned = lax.all_to_all(block_rows, "own", split_axis=0, concat_axis=0, tiled=True)
    per_slot = (
        returned.reshape(experts_here, SPLIT, 16, returned.shape[-1])
        .astype(jnp.float32)
        .sum(axis=1)
        .reshape(experts_here * CAP, model_width)
    )
    grad_tokens = jnp.dot(
        select, per_slot, precision=lax.Precision.HIGHEST, preferred_element_type=jnp.float32
    ).astype(jnp.bfloat16)
    stacked = jnp.stack([grad_gate, grad_up, grad_down]).astype(jnp.bfloat16)
    shares = lax.psum_scatter(stacked, "rep", scatter_dimension=1, tiled=True).astype(jnp.float32)
    return (grad_tokens, shares[0], shares[1], shares[2])


def solution(mesh):
    return jax.shard_map(
        per_device,
        mesh=mesh,
        in_specs=(
            P(("own", "rep"), None),
            P(("own", "rep"), None),
            P(("own", "rep"), None),
            P(("own", "rep"), None),
            P(),
            P(("own", "rep"), None),
            P(("own", "rep"), None),
            P(("own", "rep"), None),
        ),
        out_specs=(
            P(("own", "rep"), None),
            P(("own", "rep"), None),
            P(("own", "rep"), None),
            P(("own", "rep"), None),
        ),
        check_vma=False,
    )
```

```python
import jax
import jax.numpy as jnp
from jax import lax
from jax.sharding import PartitionSpec as P

SPLIT = 4
CAP = 6


def silu_parts(pre_gate):
    sigmoid_value = jax.nn.sigmoid(pre_gate)
    return (pre_gate * sigmoid_value, sigmoid_value * (1.0 + pre_gate * (1.0 - sigmoid_value)))


def panel_terms(rows_x, rows_cot, panel_gate, panel_up, panel_down):
    pre_gate = jnp.dot(rows_x, panel_gate.T, preferred_element_type=jnp.float32)
    pre_up = jnp.dot(rows_x, panel_up.T, preferred_element_type=jnp.float32)
    active, slope_value = silu_parts(pre_gate)
    hidden = (active * pre_up).astype(jnp.bfloat16)
    hidden_delta = jnp.dot(rows_cot, panel_down.T, preferred_element_type=jnp.float32)
    gate_delta = (hidden_delta * pre_up * slope_value).astype(jnp.bfloat16)
    up_delta = (hidden_delta * active).astype(jnp.bfloat16)
    grad_rows = jnp.dot(gate_delta, panel_gate, preferred_element_type=jnp.float32) + jnp.dot(
        up_delta, panel_up, preferred_element_type=jnp.float32
    )
    grad_gate = jnp.dot(gate_delta.T, rows_x, preferred_element_type=jnp.float32)
    grad_up = jnp.dot(up_delta.T, rows_x, preferred_element_type=jnp.float32)
    grad_down = jnp.dot(hidden.T, rows_cot, preferred_element_type=jnp.float32)
    return (grad_rows, grad_gate, grad_up, grad_down)


def slot_tables(route, gate_index, gate_table, experts_here):
    tok_count, choices_each = route.shape
    slots = experts_here * CAP
    column = jnp.arange(slots, dtype=jnp.int32)[None, :]
    pair_route = route.reshape(-1)[:, None]
    is_named = (pair_route == column // CAP).astype(jnp.int32)
    earlier = jnp.cumsum(is_named, axis=0) - is_named
    hit = jnp.where(earlier == column % CAP, is_named, 0)
    gate_values = jnp.take(gate_table, gate_index.reshape(-1), axis=0)
    slot_gate = jnp.sum(jnp.where(hit > 0, gate_values[:, None], 0.0), axis=0)
    select = hit.reshape(tok_count, choices_each, slots).sum(axis=1).astype(jnp.float32)
    return select, slot_gate


def per_device(tokens, cotangent, route, gate_index, gate_table, w_gate, w_up, w_down):
    owners = lax.axis_size("own")
    experts_here = owners // SPLIT
    model_width = tokens.shape[1]
    select, slot_gate = slot_tables(route, gate_index, gate_table, experts_here)
    picker = select.astype(jnp.bfloat16)
    sent_x = jnp.dot(picker.T, tokens, preferred_element_type=jnp.float32).astype(jnp.bfloat16)
    sent_dy = jnp.dot(picker.T, cotangent, preferred_element_type=jnp.float32)
    sent_cot = (slot_gate[:, None] * sent_dy).astype(jnp.bfloat16)

    full_gate, full_up, full_down = (
        lax.all_gather(w_gate, "rep", axis=0, tiled=True),
        lax.all_gather(w_up, "rep", axis=0, tiled=True),
        lax.all_gather(w_down, "rep", axis=0, tiled=True),
    )
    x_slots = sent_x.reshape(experts_here, CAP, model_width)
    cot_slots = sent_cot.reshape(experts_here, CAP, model_width)
    chunk = CAP // 2
    received = []
    for part in range(2):
        cut = slice(part * chunk, (part + 1) * chunk)
        both = jnp.concatenate([x_slots[:, cut], cot_slots[:, cut]], axis=1).reshape(
            experts_here, 1, 16, -1
        )
        spread = jnp.broadcast_to(both, (experts_here, SPLIT) + both.shape[2:]).reshape(owners, 16, -1)
        received.append(lax.all_to_all(spread, "own", split_axis=0, concat_axis=0, tiled=True))
    weight_sums = None
    slot_parts = []
    for got in received:
        rows_x = got[:, :8].reshape(owners * chunk, model_width)
        rows_cot = got[:, 8:].reshape(owners * chunk, model_width)
        grad_rows, grad_gate, grad_up, grad_down = panel_terms(
            rows_x, rows_cot, full_gate, full_up, full_down
        )
        terms = (grad_gate, grad_up, grad_down)
        weight_sums = terms if weight_sums is None else tuple(a + b for a, b in zip(weight_sums, terms))
        block_rows = grad_rows.astype(jnp.bfloat16).reshape(owners, 16, -1)
        returned = lax.all_to_all(block_rows, "own", split_axis=0, concat_axis=0, tiled=True)
        slot_parts.append(
            returned.reshape(experts_here, SPLIT, 16, returned.shape[-1])
            .astype(jnp.float32)
            .sum(axis=1)
            .reshape(experts_here, chunk, model_width)
        )
    per_slot = jnp.concatenate(slot_parts, axis=1).reshape(experts_here * CAP, model_width)
    grad_tokens = jnp.dot(
        select, per_slot, precision=lax.Precision.HIGHEST, preferred_element_type=jnp.float32
    ).astype(jnp.bfloat16)
    stacked = jnp.stack(weight_sums).astype(jnp.bfloat16)
    shares = lax.psum_scatter(stacked, "rep", scatter_dimension=1, tiled=True).astype(jnp.float32)
    return (grad_tokens, shares[0], shares[1], shares[2])


def solution(mesh):
    return jax.shard_map(
        per_device,
        mesh=mesh,
        in_specs=(
            P(("own", "rep"), None),
            P(("own", "rep"), None),
            P(("own", "rep"), None),
            P(("own", "rep"), None),
            P(),
            P(("own", "rep"), None),
            P(("own", "rep"), None),
            P(("own", "rep"), None),
        ),
        out_specs=(
            P(("own", "rep"), None),
            P(("own", "rep"), None),
            P(("own", "rep"), None),
            P(("own", "rep"), None),
        ),
        check_vma=False,
    )
```

```python
import jax
import jax.numpy as jnp
from jax import lax
from jax.sharding import PartitionSpec as P

SPLIT = 4
CAP = 6


def silu_parts(pre_gate):
    sigmoid_value = jax.nn.sigmoid(pre_gate)
    return (pre_gate * sigmoid_value, sigmoid_value * (1.0 + pre_gate * (1.0 - sigmoid_value)))


def panel_terms(rows_x, rows_cot, panel_gate, panel_up, panel_down):
    pre_gate = jnp.dot(rows_x, panel_gate.T, preferred_element_type=jnp.float32)
    pre_up = jnp.dot(rows_x, panel_up.T, preferred_element_type=jnp.float32)
    active, slope_value = silu_parts(pre_gate)
    hidden = (active * pre_up).astype(jnp.bfloat16)
    hidden_delta = jnp.dot(rows_cot, panel_down.T, preferred_element_type=jnp.float32)
    gate_delta = (hidden_delta * pre_up * slope_value).astype(jnp.bfloat16)
    up_delta = (hidden_delta * active).astype(jnp.bfloat16)
    grad_rows = jnp.dot(gate_delta, panel_gate, preferred_element_type=jnp.float32) + jnp.dot(
        up_delta, panel_up, preferred_element_type=jnp.float32
    )
    grad_gate = jnp.dot(gate_delta.T, rows_x, preferred_element_type=jnp.float32)
    grad_up = jnp.dot(up_delta.T, rows_x, preferred_element_type=jnp.float32)
    grad_down = jnp.dot(hidden.T, rows_cot, preferred_element_type=jnp.float32)
    return (grad_rows, grad_gate, grad_up, grad_down)


def slot_tables(route, gate_index, gate_table, experts_here):
    tok_count, choices_each = route.shape
    slots = experts_here * CAP
    column = jnp.arange(slots, dtype=jnp.int32)[None, :]
    pair_route = route.reshape(-1)[:, None]
    is_named = (pair_route == column // CAP).astype(jnp.int32)
    earlier = jnp.cumsum(is_named, axis=0) - is_named
    hit = jnp.where(earlier == column % CAP, is_named, 0)
    slot_entry = jnp.sum(jnp.where(hit > 0, gate_index.reshape(-1)[:, None], 0), axis=0)
    table_ids = jnp.arange(gate_table.shape[0], dtype=jnp.int32)[None, :]
    slot_gate = jnp.sum(jnp.where(slot_entry[:, None] == table_ids, gate_table[None, :], 0.0), axis=1)
    select = hit.reshape(tok_count, choices_each, slots).sum(axis=1).astype(jnp.float32)
    return select, slot_gate


def per_device(tokens, cotangent, route, gate_index, gate_table, w_gate, w_up, w_down):
    owners = lax.axis_size("own")
    experts_here = owners // SPLIT
    model_width = tokens.shape[1]
    select, slot_gate = slot_tables(route, gate_index, gate_table, experts_here)
    picker = select.astype(jnp.bfloat16)
    sent_x = jnp.dot(picker.T, tokens, preferred_element_type=jnp.float32).astype(jnp.bfloat16)
    sent_dy = jnp.dot(picker.T, cotangent, preferred_element_type=jnp.float32)
    sent_cot = (slot_gate[:, None] * sent_dy).astype(jnp.bfloat16)

    both = jnp.concatenate(
        [sent_x.reshape(experts_here, CAP, model_width), sent_cot.reshape(experts_here, CAP, model_width)],
        axis=1,
    ).reshape(experts_here, 1, 16, -1)
    spread = jnp.broadcast_to(both, (experts_here, SPLIT) + both.shape[2:]).reshape(owners, 16, -1)
    got = lax.all_to_all(spread, "own", split_axis=0, concat_axis=0, tiled=True)
    rows_x = got[:, :8].reshape(owners * CAP, model_width)
    rows_cot = got[:, 8:].reshape(owners * CAP, model_width)
    full_gate, full_up, full_down = (
        lax.all_gather(w_gate, "rep", axis=0, tiled=True),
        lax.all_gather(w_up, "rep", axis=0, tiled=True),
        lax.all_gather(w_down, "rep", axis=0, tiled=True),
    )
    grad_rows, grad_gate, grad_up, grad_down = panel_terms(
        rows_x, rows_cot, full_gate, full_up, full_down
    )
    block_rows = grad_rows.astype(jnp.bfloat16).reshape(owners, 16, -1)
    returned = lax.all_to_all(block_rows, "own", split_axis=0, concat_axis=0, tiled=True)
    per_slot = (
        returned.reshape(experts_here, SPLIT, 16, returned.shape[-1])
        .astype(jnp.float32)
        .sum(axis=1)
        .reshape(experts_here * CAP, model_width)
    )
    grad_tokens = jnp.dot(
        select, per_slot, precision=lax.Precision.HIGHEST, preferred_element_type=jnp.float32
    ).astype(jnp.bfloat16)
    stacked = jnp.stack([grad_gate, grad_up, grad_down]).astype(jnp.bfloat16)
    shares = lax.psum_scatter(stacked, "rep", scatter_dimension=1, tiled=True).astype(jnp.float32)
    return (grad_tokens, shares[0], shares[1], shares[2])


def solution(mesh):
    return jax.shard_map(
        per_device,
        mesh=mesh,
        in_specs=(
            P(("own", "rep"), None),
            P(("own", "rep"), None),
            P(("own", "rep"), None),
            P(("own", "rep"), None),
            P(),
            P(("own", "rep"), None),
            P(("own", "rep"), None),
            P(("own", "rep"), None),
        ),
        out_specs=(
            P(("own", "rep"), None),
            P(("own", "rep"), None),
            P(("own", "rep"), None),
            P(("own", "rep"), None),
        ),
        check_vma=False,
    )
```

```python
import jax
import jax.numpy as jnp
from jax import lax
from jax.sharding import PartitionSpec as P

SPLIT = 4
CAP = 6


def silu_parts(pre_gate):
    sigmoid_value = jax.nn.sigmoid(pre_gate)
    return (pre_gate * sigmoid_value, sigmoid_value * (1.0 + pre_gate * (1.0 - sigmoid_value)))


def panel_terms(rows_x, rows_cot, panel_gate, panel_up, panel_down):
    pre_gate = jnp.dot(rows_x, panel_gate.T, preferred_element_type=jnp.float32)
    pre_up = jnp.dot(rows_x, panel_up.T, preferred_element_type=jnp.float32)
    active, slope_value = silu_parts(pre_gate)
    hidden = (active * pre_up).astype(jnp.bfloat16)
    hidden_delta = jnp.dot(rows_cot, panel_down.T, preferred_element_type=jnp.float32)
    gate_delta = (hidden_delta * pre_up * slope_value).astype(jnp.bfloat16)
    up_delta = (hidden_delta * active).astype(jnp.bfloat16)
    grad_rows = jnp.dot(gate_delta, panel_gate, preferred_element_type=jnp.float32) + jnp.dot(
        up_delta, panel_up, preferred_element_type=jnp.float32
    )
    grad_gate = jnp.dot(gate_delta.T, rows_x, preferred_element_type=jnp.float32)
    grad_up = jnp.dot(up_delta.T, rows_x, preferred_element_type=jnp.float32)
    grad_down = jnp.dot(hidden.T, rows_cot, preferred_element_type=jnp.float32)
    return (grad_rows, grad_gate, grad_up, grad_down)


def slot_tables(route, gate_index, gate_table, experts_here):
    tok_count, choices_each = route.shape
    slots = experts_here * CAP
    column = jnp.arange(slots, dtype=jnp.int32)[None, :]
    pair_route = route.reshape(-1)[:, None]
    is_named = (pair_route == column // CAP).astype(jnp.int32)
    earlier = jnp.cumsum(is_named, axis=0) - is_named
    hit = jnp.where(earlier == column % CAP, is_named, 0)
    slot_entry = jnp.sum(jnp.where(hit > 0, gate_index.reshape(-1)[:, None], 0), axis=0)
    table_ids = jnp.arange(gate_table.shape[0], dtype=jnp.int32)[None, :]
    slot_gate = jnp.sum(jnp.where(slot_entry[:, None] == table_ids, gate_table[None, :], 0.0), axis=1)
    select = hit.reshape(tok_count, choices_each, slots).sum(axis=1).astype(jnp.float32)
    return select, slot_gate


def per_device(tokens, cotangent, route, gate_index, gate_table, w_gate, w_up, w_down):
    owners = lax.axis_size("own")
    experts_here = owners // SPLIT
    model_width = tokens.shape[1]
    select, slot_gate = slot_tables(route, gate_index, gate_table, experts_here)
    picker = select.astype(jnp.bfloat16)
    sent_x = jnp.dot(picker.T, tokens, preferred_element_type=jnp.float32).astype(jnp.bfloat16)
    sent_dy = jnp.dot(picker.T, cotangent, preferred_element_type=jnp.float32)
    sent_cot = (slot_gate[:, None] * sent_dy).astype(jnp.bfloat16)

    both = jnp.concatenate(
        [sent_x.reshape(experts_here, CAP, model_width), sent_cot.reshape(experts_here, CAP, model_width)],
        axis=1,
    ).reshape(experts_here, 1, 16, -1)
    spread = jnp.broadcast_to(both, (experts_here, SPLIT) + both.shape[2:]).reshape(owners, 16, -1)
    got = lax.all_to_all(spread, "own", split_axis=0, concat_axis=0, tiled=True)
    rows_x = got[:, :8].reshape(owners * CAP, model_width)
    rows_cot = got[:, 8:].reshape(owners * CAP, model_width)
    full_gate, full_up, full_down = (
        lax.all_gather(w_gate, "rep", axis=0, tiled=True),
        lax.all_gather(w_up, "rep", axis=0, tiled=True),
        lax.all_gather(w_down, "rep", axis=0, tiled=True),
    )
    grad_rows, grad_gate, grad_up, grad_down = panel_terms(
        rows_x, rows_cot, full_gate, full_up, full_down
    )
    block_rows = grad_rows.astype(jnp.bfloat16).reshape(owners, 16, -1)
    returned = lax.all_to_all(block_rows, "own", split_axis=0, concat_axis=0, tiled=True)
    per_slot = (
        returned.reshape(experts_here, SPLIT, 16, returned.shape[-1])
        .astype(jnp.float32)
        .sum(axis=1)
        .reshape(experts_here * CAP, model_width)
    )
    grad_tokens = jnp.dot(
        select, per_slot, precision=lax.Precision.HIGHEST, preferred_element_type=jnp.float32
    ).astype(jnp.bfloat16)
    partials = tuple(g.astype(jnp.bfloat16) for g in (grad_gate, grad_up, grad_down))
    shares = lax.psum_scatter(partials, "rep", scatter_dimension=0, tiled=True)
    return (grad_tokens,) + tuple(share.astype(jnp.float32) for share in shares)


def solution(mesh):
    return jax.shard_map(
        per_device,
        mesh=mesh,
        in_specs=(
            P(("own", "rep"), None),
            P(("own", "rep"), None),
            P(("own", "rep"), None),
            P(("own", "rep"), None),
            P(),
            P(("own", "rep"), None),
            P(("own", "rep"), None),
            P(("own", "rep"), None),
        ),
        out_specs=(
            P(("own", "rep"), None),
            P(("own", "rep"), None),
            P(("own", "rep"), None),
            P(("own", "rep"), None),
        ),
        check_vma=False,
    )
```

```python
import jax
import jax.numpy as jnp
from jax import lax
from jax.sharding import PartitionSpec as P

SPLIT = 4
CAP = 6


def silu_parts(pre_gate):
    sigmoid_value = jax.nn.sigmoid(pre_gate)
    return (pre_gate * sigmoid_value, sigmoid_value * (1.0 + pre_gate * (1.0 - sigmoid_value)))


def panel_terms(rows_x, rows_cot, panel_gate, panel_up, panel_down):
    pre_gate = jnp.dot(rows_x, panel_gate.T, preferred_element_type=jnp.float32)
    pre_up = jnp.dot(rows_x, panel_up.T, preferred_element_type=jnp.float32)
    active, slope_value = silu_parts(pre_gate)
    hidden = (active * pre_up).astype(jnp.bfloat16)
    hidden_delta = jnp.dot(rows_cot, panel_down.T, preferred_element_type=jnp.float32)
    gate_delta = (hidden_delta * pre_up * slope_value).astype(jnp.bfloat16)
    up_delta = (hidden_delta * active).astype(jnp.bfloat16)
    grad_rows = jnp.dot(gate_delta, panel_gate, preferred_element_type=jnp.float32) + jnp.dot(
        up_delta, panel_up, preferred_element_type=jnp.float32
    )
    grad_gate = jnp.dot(gate_delta.T, rows_x, preferred_element_type=jnp.float32)
    grad_up = jnp.dot(up_delta.T, rows_x, preferred_element_type=jnp.float32)
    grad_down = jnp.dot(hidden.T, rows_cot, preferred_element_type=jnp.float32)
    return (grad_rows, grad_gate, grad_up, grad_down)


def slot_tables(route, gate_index, gate_table, experts_here):
    tok_count, choices_each = route.shape
    slots = experts_here * CAP
    column = jnp.arange(slots, dtype=jnp.int32)[None, :]
    pair_route = route.reshape(-1)[:, None]
    is_named = (pair_route == column // CAP).astype(jnp.int32)
    earlier = jnp.cumsum(is_named, axis=0) - is_named
    hit = jnp.where(earlier == column % CAP, is_named, 0)
    slot_entry = jnp.sum(jnp.where(hit > 0, gate_index.reshape(-1)[:, None], 0), axis=0)
    table_ids = jnp.arange(gate_table.shape[0], dtype=jnp.int32)[None, :]
    slot_gate = jnp.sum(jnp.where(slot_entry[:, None] == table_ids, gate_table[None, :], 0.0), axis=1)
    select = hit.reshape(tok_count, choices_each, slots).sum(axis=1).astype(jnp.float32)
    return select, slot_gate


def per_device(tokens, cotangent, route, gate_index, gate_table, w_gate, w_up, w_down):
    owners = lax.axis_size("own")
    experts_here = owners // SPLIT
    model_width = tokens.shape[1]
    select, slot_gate = slot_tables(route, gate_index, gate_table, experts_here)
    picker = select.astype(jnp.bfloat16)
    sent_x = jnp.dot(picker.T, tokens, preferred_element_type=jnp.float32).astype(jnp.bfloat16)
    sent_dy = jnp.dot(picker.T, cotangent, preferred_element_type=jnp.float32)
    sent_cot = (slot_gate[:, None] * sent_dy).astype(jnp.bfloat16)

    both = jnp.concatenate(
        [sent_x.reshape(experts_here, CAP, model_width), sent_cot.reshape(experts_here, CAP, model_width)],
        axis=1,
    ).reshape(experts_here, 1, 16, -1)
    spread = jnp.broadcast_to(both, (experts_here, SPLIT) + both.shape[2:]).reshape(owners, 16, -1)
    got = lax.all_to_all(spread, "own", split_axis=0, concat_axis=0, tiled=True)
    rows_x = got[:, :8].reshape(owners * CAP, model_width)
    rows_cot = got[:, 8:].reshape(owners * CAP, model_width)
    full_gate, full_up, full_down = (
        lax.all_gather(w_gate, "rep", axis=0, tiled=True),
        lax.all_gather(w_up, "rep", axis=0, tiled=True),
        lax.all_gather(w_down, "rep", axis=0, tiled=True),
    )
    grad_rows, grad_gate, grad_up, grad_down = panel_terms(
        rows_x, rows_cot, full_gate, full_up, full_down
    )
    block_rows = grad_rows.astype(jnp.bfloat16).reshape(owners, 16, -1)
    returned = lax.all_to_all(block_rows, "own", split_axis=0, concat_axis=0, tiled=True)
    per_slot = (
        returned.reshape(experts_here, SPLIT, 16, returned.shape[-1])
        .astype(jnp.float32)
        .sum(axis=1)
        .reshape(experts_here * CAP, model_width)
    )
    grad_tokens = jnp.dot(
        select, per_slot, precision=lax.Precision.HIGHEST, preferred_element_type=jnp.float32
    ).astype(jnp.bfloat16)
    stacked = jnp.stack([grad_gate, grad_up, grad_down]).astype(jnp.bfloat16)
    shares = lax.psum_scatter(stacked, "rep", scatter_dimension=1, tiled=True)
    return (grad_tokens,) + tuple(shares[i].astype(jnp.float32) for i in range(3))


def solution(mesh):
    return jax.shard_map(
        per_device,
        mesh=mesh,
        in_specs=(
            P(("own", "rep"), None),
            P(("own", "rep"), None),
            P(("own", "rep"), None),
            P(("own", "rep"), None),
            P(),
            P(("own", "rep"), None),
            P(("own", "rep"), None),
            P(("own", "rep"), None),
        ),
        out_specs=(
            P(("own", "rep"), None),
            P(("own", "rep"), None),
            P(("own", "rep"), None),
            P(("own", "rep"), None),
        ),
        check_vma=False,
    )
```
